256 devices in a mesh: doc: 8 (over y, core), seq: 32 (over z, x).
Axes of the slice: x: 4, y: 4, z: 8, core: 2. Of those that a mesh axis runs over, the one named last changes fastest.
Arguments:
- queries: bfloat16 [163840, 4096], P(('doc', 'seq')), parts along dimension 0, may hold values from -75 to 75
- memory_kv: bfloat16 [256, 384, 1024], P(('doc', 'seq')), parts along dimension 0, may hold values from -8 to 8
- block_image: int32 [1280], P(('doc', 'seq')), parts along dimension 0, may hold values from -1 to 31
- image_slot: int32 [256], P('doc'), parts along dimension 0, may hold values from 0 to 31, each once
Outputs:
- context: bfloat16 [163840, 4096], P(('doc', 'seq')), parts along dimension 0
The draws below stay inside these ranges and needn't reach their ends.
There are 8 independent parts, one for each index of `doc`. The reference program is written for one: setup_inputs(seed, part) draws one part's arguments, and reference() takes and returns one part's arrays. A program takes and returns all parts, laid end to end along the dimension named above; each array names one. Nothing has to cross between parts.
Inputs may be any that keep to these rules, and one draw needn't show every extreme that they name: `block_image`: -1 marks a block without an image. A permutation: image i is held by seq index image_slot[i].
All inputs are finite; a program needn't handle non-finite values.
Results may differ from the reference program's by a relative error of at most 0.0049.
Values may be sent and summed in bfloat16 or wider, within the bound.
No kernel may reach another device: no remote copies, remote signals or barrier semaphores. Data moves between devices by JAX's collectives and lax.ppermute only.
A program may use at most 192 MiB of HBM per device.

```python
import jax
import jax.numpy as jnp
from jax import lax

HD = 128
HEADS = 32
KV_HEADS = 4
BLOCK = 128
IMG_TOK = 384
SEQ_LEN = 20480
BLOCKS = 160
IMAGES = 32


def draw_queries(key, part):
    base = jnp.clip(jax.random.normal(jax.random.fold_in(key, 1), (SEQ_LEN, HEADS, HD), jnp.float32), -6.0, 6.0)
    return base.reshape(SEQ_LEN, HEADS * HD).astype(jnp.bfloat16)


def draw_memory_kv(key, part):
    base = jnp.clip(jax.random.normal(jax.random.fold_in(key, 3), (IMAGES, IMG_TOK, KV_HEADS, 2, HD), jnp.float32), -6.0, 6.0)
    return base.reshape(IMAGES, IMG_TOK, KV_HEADS * 2 * HD).astype(jnp.bfloat16)


def plant(values, own_key, smallest, top_value):
    dims = values.shape
    spot = [jax.random.randint(jax.random.fold_in(own_key, axis), (), 0, dims[axis]) for axis in range(len(dims))]
    values = values.at[tuple(spot)].set(smallest)
    longest = dims.index(max(dims))
    spot[longest] = (spot[longest] + 1) % dims[longest]
    return values.at[tuple(spot)].set(top_value)


def setup_inputs(seed: int = 0, part: int = 0) -> dict:
    keys = jax.random.split(jax.random.key(seed), 5)
    own_keys = jax.random.split(jax.random.fold_in(keys[4], part), 5)
    queries = draw_queries(jax.random.fold_in(jax.random.fold_in(keys[4], part), 71), part)
    memory_kv = draw_memory_kv(jax.random.fold_in(jax.random.fold_in(keys[4], part), 71), part)
    block_image = plant(jax.random.randint(own_keys[2], (BLOCKS,), -1, IMAGES), jax.random.fold_in(own_keys[2], 1), -1, IMAGES - 1).astype(jnp.int32)
    image_slot = jax.random.permutation(own_keys[3], IMAGES).astype(jnp.int32)
    return {"queries": queries, "memory_kv": memory_kv, "block_image": block_image, "image_slot": image_slot}


def block_attention(query_block, image_id, memory_kv, image_slot):
    group_size = HEADS // KV_HEADS
    safe_image = jnp.maximum(image_id, 0).astype(jnp.int32)
    held_slot = image_slot[safe_image].astype(jnp.int32)
    memory_rows = lax.dynamic_index_in_dim(memory_kv, held_slot, 0, keepdims=False)
    memory_rows = memory_rows.astype(jnp.float32).reshape(IMG_TOK, KV_HEADS, 2, HD)
    query_heads = query_block.astype(jnp.float32).reshape(BLOCK, KV_HEADS, group_size, HD)
    scores = jnp.einsum("rhgd,khd->hgrk", query_heads, memory_rows[:, :, 0]) * (HD ** -0.5)
    row_max = jnp.max(scores, axis=-1, keepdims=True)
    weights = jnp.exp(scores - row_max)
    attn_weights = (weights / jnp.sum(weights, axis=-1, keepdims=True)).astype(jnp.bfloat16)
    attn_weights = lax.optimization_barrier(attn_weights).astype(jnp.float32)
    context = jnp.einsum("hgrk,khd->rhgd", attn_weights, memory_rows[:, :, 1])
    context = jnp.where(image_id >= 0, context, 0.0)
    return context.reshape(BLOCK, HEADS * HD).astype(jnp.bfloat16)


def reference(queries, memory_kv, block_image, image_slot):
    blocks = queries.reshape(BLOCKS, BLOCK, HEADS * HD)
    result = lax.map(lambda pair: block_attention(pair[0], pair[1], memory_kv, image_slot), (blocks, block_image))
    return result.reshape(SEQ_LEN, HEADS * HD)
```

```python
import functools

import jax
import jax.numpy as jnp
from jax import lax
from jax.experimental import pallas as pl
from jax.experimental.pallas import tpu as pltpu
from jax.sharding import PartitionSpec as P

HD = 128
KV_HEADS = 4
BLOCK = 128
ROW_GROUPS = 8


def attend_kernel(image_ref, q_ref, kv_ref, o_ref, *, group_size, memory_rows):
    b = pl.program_id(0)
    kv = kv_ref[...].reshape(memory_rows, 2 * HD)
    k = kv[:, :HD]
    v = kv[:, HD:]
    valid = image_ref[b] >= 0
    for g in range(group_size):
        q = q_ref[:, g * HD:(g + 1) * HD]
        s = lax.dot_general(q, k, (((1,), (1,)), ((), ())), preferred_element_type=jnp.float32)
        s = s * HD ** (-0.5)
        m = jnp.max(s, axis=-1, keepdims=True)
        w = jnp.exp(s - m)
        inv = 1.0 / jnp.sum(w, axis=-1, keepdims=True)
        p = (w * inv).astype(jnp.bfloat16)
        ctx = jnp.dot(p, v, preferred_element_type=jnp.float32)
        ctx = jnp.where(valid, ctx, 0.0)
        o_ref[:, g * HD:(g + 1) * HD] = ctx.astype(o_ref.dtype)


def attend(queries, kv_shares, block_image):
    row_count, row_width = queries.shape
    _, kv_local, count_blocks, share_rows, _ = kv_shares.shape
    group_size = row_width // (HD * kv_local)
    head_cols = group_size * HD
    kernel = functools.partial(
        attend_kernel, group_size=group_size, memory_rows=ROW_GROUPS * share_rows
    )
    grid_spec = pltpu.PrefetchScalarGridSpec(
        num_scalar_prefetch=1,
        grid=(count_blocks, kv_local),
        in_specs=[
            pl.BlockSpec((BLOCK, head_cols), lambda b, j, img: (b, j)),
            pl.BlockSpec(
                (ROW_GROUPS, None, None, share_rows, 2 * HD),
                lambda b, j, img: (0, j, b, 0, 0),
            ),
        ],
        out_specs=pl.BlockSpec((BLOCK, head_cols), lambda b, j, img: (b, j)),
    )
    return pl.pallas_call(
        kernel,
        grid_spec=grid_spec,
        out_shape=jax.ShapeDtypeStruct(queries.shape, queries.dtype),
    )(block_image, queries, kv_shares)


def local(queries, memory_kv, block_image, image_slot):
    seq_count = lax.axis_size("seq")
    own_blocks = block_image.shape[0]
    _, img_rows, kv_width = memory_kv.shape
    kv_local = kv_width // (2 * HD)
    share_rows = img_rows // ROW_GROUPS
    shares = memory_kv.reshape(ROW_GROUPS, share_rows, kv_local, 2 * HD)
    shares = shares.transpose(0, 2, 1, 3).reshape(seq_count, share_rows, 2 * HD)
    wanted = lax.all_gather(block_image, "seq", axis=0, tiled=True)
    held = lax.all_to_all(shares, "seq", split_axis=0, concat_axis=0, tiled=True)
    wanted_slot = jnp.take(image_slot, jnp.maximum(wanted, 0), axis=0)
    outgoing = jnp.take(held, wanted_slot, axis=0)
    outgoing = outgoing.reshape(seq_count, own_blocks, share_rows, 2 * HD)
    arrived = lax.all_to_all(outgoing, "seq", split_axis=0, concat_axis=0, tiled=True)
    arrived = arrived.reshape(ROW_GROUPS, kv_local, own_blocks, share_rows, 2 * HD)
    return attend(queries, arrived, block_image)


def solution(mesh):
    placed = (P(("doc", "seq"), None), P(("doc", "seq"), None, None), P(("doc", "seq")), P("doc"))
    return jax.shard_map(
        local, mesh=mesh, in_specs=placed, out_specs=P(("doc", "seq"), None), check_vma=False
    )
```

```python
import functools

import jax
import jax.numpy as jnp
from jax import lax
from jax.experimental import pallas as pl
from jax.experimental.pallas import tpu as pltpu
from jax.sharding import PartitionSpec as P

HD = 128
KV_HEADS = 4
BLOCK = 128
ROW_GROUPS = 8
TAG_ROWS = 16


def attend_kernel(image_ref, q_ref, kv_ref, o_ref, *, group_size, memory_rows):
    b = pl.program_id(0)
    kv = kv_ref[...].reshape(memory_rows, 2 * HD)
    k = kv[:, :HD]
    v = kv[:, HD:]
    valid = image_ref[b] >= 0
    q = jnp.concatenate([q_ref[:, g * HD:(g + 1) * HD] for g in range(group_size)], axis=0)
    s = lax.dot_general(k, q, (((1,), (1,)), ((), ())), preferred_element_type=jnp.float32)
    s = s * HD ** (-0.5)
    m = jnp.max(s, axis=0, keepdims=True)
    w = jnp.exp(s - m)
    inv = 1.0 / jnp.sum(w, axis=0, keepdims=True)
    p = (w * inv).astype(jnp.bfloat16)
    ctx = lax.dot_general(p, v, (((0,), (0,)), ((), ())), preferred_element_type=jnp.float32)
    ctx = jnp.where(valid, ctx, 0.0).astype(o_ref.dtype)
    for g in range(group_size):
        o_ref[:, g * HD:(g + 1) * HD] = ctx[g * BLOCK:(g + 1) * BLOCK]


def attend(queries, kv_shares, block_image):
    row_count, row_width = queries.shape
    _, kv_local, count_blocks, share_rows, _ = kv_shares.shape
    group_size = row_width // (HD * kv_local)
    head_cols = group_size * HD
    kernel = functools.partial(
        attend_kernel, group_size=group_size, memory_rows=ROW_GROUPS * share_rows
    )
    grid_spec = pltpu.PrefetchScalarGridSpec(
        num_scalar_prefetch=1,
        grid=(count_blocks, kv_local),
        in_specs=[
            pl.BlockSpec((BLOCK, head_cols), lambda b, j, img: (b, j)),
            pl.BlockSpec(
                (ROW_GROUPS, None, None, share_rows, 2 * HD),
                lambda b, j, img: (0, j, b, 0, 0),
            ),
        ],
        out_specs=pl.BlockSpec((BLOCK, head_cols), lambda b, j, img: (b, j)),
    )
    return pl.pallas_call(
        kernel,
        grid_spec=grid_spec,
        out_shape=jax.ShapeDtypeStruct(queries.shape, queries.dtype),
    )(block_image, queries, kv_shares)


def holder_of(image_ids, image_slot):
    image_count = image_slot.shape[0]
    same_image = image_ids[:, None] == jnp.arange(image_count, dtype=jnp.int32)[None, :]
    return jnp.sum(jnp.where(same_image, image_slot[None, :], 0), axis=1)


def local(queries, memory_kv, block_image, image_slot):
    seq_count = lax.axis_size("seq")
    own_blocks = block_image.shape[0]
    _, img_rows, kv_width = memory_kv.shape
    kv_local = kv_width // (2 * HD)
    share_rows = img_rows // ROW_GROUPS
    shares = memory_kv.reshape(ROW_GROUPS, share_rows, kv_local, 2 * HD)
    shares = shares.transpose(0, 2, 1, 3).reshape(seq_count, share_rows, 2 * HD)
    tag = jnp.zeros((seq_count, TAG_ROWS, 2 * HD), shares.dtype)
    tag = tag.at[:, 0, :own_blocks].set(block_image.astype(shares.dtype)[None, :])
    payload = jnp.concatenate([shares, tag], axis=1)
    held = lax.all_to_all(payload, "seq", split_axis=0, concat_axis=0, tiled=True)
    wanted = held[:, share_rows, :own_blocks].astype(jnp.int32).reshape(seq_count * own_blocks)
    wanted_slot = holder_of(wanted, image_slot)
    outgoing = jnp.take(held[:, :share_rows], wanted_slot, axis=0, mode="clip")
    outgoing = outgoing.reshape(seq_count, own_blocks, share_rows, 2 * HD)
    arrived = lax.all_to_all(outgoing, "seq", split_axis=0, concat_axis=0, tiled=True)
    arrived = arrived.reshape(ROW_GROUPS, kv_local, own_blocks, share_rows, 2 * HD)
    return attend(queries, arrived, block_image)


def solution(mesh):
    placed = (P(("doc", "seq"), None), P(("doc", "seq"), None, None), P(("doc", "seq")), P("doc"))
    return jax.shard_map(
        local, mesh=mesh, in_specs=placed, out_specs=P(("doc", "seq"), None), check_vma=False
    )
```

```python
import functools

import jax
import jax.numpy as jnp
from jax import lax
from jax.experimental import pallas as pl
from jax.experimental.pallas import tpu as pltpu
from jax.sharding import PartitionSpec as P

HD = 128
KV_HEADS = 4
BLOCK = 128
ROW_GROUPS = 8
TAG_ROWS = 16
LOG2E = 1.4426950408889634


def attend_head(q_ref, kv, o_ref, valid, col0, group_size):
    k = kv[:, :HD]
    v = kv[:, HD:]
    q = jnp.concatenate(
        [q_ref[:, col0 + g * HD:col0 + (g + 1) * HD] for g in range(group_size)], axis=0
    )
    s = lax.dot_general(k, q, (((1,), (1,)), ((), ())), preferred_element_type=jnp.float32)
    m = jnp.max(s, axis=0, keepdims=True)
    w = jnp.exp2((s - m) * (HD ** (-0.5) * LOG2E))
    inv = 1.0 / jnp.sum(w, axis=0, keepdims=True)
    p = (w * inv).astype(jnp.bfloat16)
    ctx = lax.dot_general(p, v, (((0,), (0,)), ((), ())), preferred_element_type=jnp.float32)
    ctx = jnp.where(valid, ctx, 0.0).astype(o_ref.dtype)
    for g in range(group_size):
        o_ref[:, col0 + g * HD:col0 + (g + 1) * HD] = ctx[g * BLOCK:(g + 1) * BLOCK]


def attend_kernel(image_ref, q_ref, kv_ref, o_ref, *, group_size, kv_local, memory_rows):
    b = pl.program_id(0)
    valid = image_ref[b] >= 0
    for j in range(kv_local):
        kv = kv_ref[:, j].reshape(memory_rows, 2 * HD)
        attend_head(q_ref, kv, o_ref, valid, j * group_size * HD, group_size)


def attend(queries, kv_shares, block_image):
    row_count, row_width = queries.shape
    _, kv_local, count_blocks, share_rows, _ = kv_shares.shape
    group_size = row_width // (HD * kv_local)
    kernel = functools.partial(
        attend_kernel, group_size=group_size, kv_local=kv_local,
        memory_rows=ROW_GROUPS * share_rows,
    )
    grid_spec = pltpu.PrefetchScalarGridSpec(
        num_scalar_prefetch=1,
        grid=(count_blocks,),
        in_specs=[
            pl.BlockSpec((BLOCK, row_width), lambda b, img: (b, 0)),
            pl.BlockSpec(
                (ROW_GROUPS, kv_local, None, share_rows, 2 * HD),
                lambda b, img: (0, 0, b, 0, 0),
            ),
        ],
        out_specs=pl.BlockSpec((BLOCK, row_width), lambda b, img: (b, 0)),
    )
    return pl.pallas_call(
        kernel,
        grid_spec=grid_spec,
        out_shape=jax.ShapeDtypeStruct(queries.shape, queries.dtype),
    )(block_image, queries, kv_shares)


def holder_of(image_ids, image_slot):
    image_count = image_slot.shape[0]
    same_image = image_ids[:, None] == jnp.arange(image_count, dtype=jnp.int32)[None, :]
    return jnp.sum(jnp.where(same_image, image_slot[None, :], 0), axis=1)


def local(queries, memory_kv, block_image, image_slot):
    seq_count = lax.axis_size("seq")
    own_blocks = block_image.shape[0]
    _, img_rows, kv_width = memory_kv.shape
    kv_local = kv_width // (2 * HD)
    share_rows = img_rows // ROW_GROUPS
    shares = memory_kv.reshape(ROW_GROUPS, share_rows, kv_local, 2 * HD)
    shares = shares.transpose(0, 2, 1, 3).reshape(seq_count, share_rows, 2 * HD)
    tag = jnp.zeros((seq_count, TAG_ROWS, 2 * HD), shares.dtype)
    tag = tag.at[:, 0, :own_blocks].set(block_image.astype(shares.dtype)[None, :])
    payload = jnp.concatenate([shares, tag], axis=1)
    held = lax.all_to_all(payload, "seq", split_axis=0, concat_axis=0, tiled=True)
    wanted = held[:, share_rows, :own_blocks].astype(jnp.int32).reshape(seq_count * own_blocks)
    wanted_slot = holder_of(wanted, image_slot)
    outgoing = jnp.take(held[:, :share_rows], wanted_slot, axis=0, mode="clip")
    outgoing = outgoing.reshape(seq_count, own_blocks, share_rows, 2 * HD)
    arrived = lax.all_to_all(outgoing, "seq", split_axis=0, concat_axis=0, tiled=True)
    arrived = arrived.reshape(ROW_GROUPS, kv_local, own_blocks, share_rows, 2 * HD)
    return attend(queries, arrived, block_image)


def solution(mesh):
    placed = (P(("doc", "seq"), None), P(("doc", "seq"), None, None), P(("doc", "seq")), P("doc"))
    return jax.shard_map(
        local, mesh=mesh, in_specs=placed, out_specs=P(("doc", "seq"), None), check_vma=False
    )
```

```python
import functools

import jax
import jax.numpy as jnp
from jax import lax
from jax.experimental import pallas as pl
from jax.experimental.pallas import tpu as pltpu
from jax.sharding import PartitionSpec as P

HD = 128
KV_HEADS = 4
BLOCK = 128
TAG_ROWS = 16
LOG2E = 1.4426950408889634


def attend_head(q_ref, k, v, o_ref, valid, col0, group_size):
    q = jnp.concatenate(
        [q_ref[:, col0 + g * HD:col0 + (g + 1) * HD] for g in range(group_size)], axis=0
    )
    s = lax.dot_general(k, q, (((1,), (1,)), ((), ())), preferred_element_type=jnp.float32)
    m = jnp.max(s, axis=0, keepdims=True)
    w = jnp.exp2((s - m) * (HD ** (-0.5) * LOG2E))
    inv = 1.0 / jnp.sum(w, axis=0, keepdims=True)
    p = (w * inv).astype(jnp.bfloat16)
    ctx = lax.dot_general(p, v, (((0,), (0,)), ((), ())), preferred_element_type=jnp.float32)
    ctx = jnp.where(valid, ctx, 0.0).astype(o_ref.dtype)
    for g in range(group_size):
        o_ref[:, col0 + g * HD:col0 + (g + 1) * HD] = ctx[g * BLOCK:(g + 1) * BLOCK]


def attend_kernel(image_ref, q_ref, kv_ref, o_ref, *, group_size, kv_local, memory_rows):
    b = pl.program_id(0)
    valid = image_ref[b] >= 0
    for j in range(kv_local):
        k = kv_ref[j, 0].reshape(memory_rows, HD)
        v = kv_ref[j, 1].reshape(memory_rows, HD)
        attend_head(q_ref, k, v, o_ref, valid, j * group_size * HD, group_size)


def attend(queries, kv_shares, block_image):
    row_count, row_width = queries.shape
    kv_local, _, row_groups, count_blocks, share_rows, _ = kv_shares.shape
    group_size = row_width // (HD * kv_local)
    kernel = functools.partial(
        attend_kernel, group_size=group_size, kv_local=kv_local,
        memory_rows=row_groups * share_rows,
    )
    grid_spec = pltpu.PrefetchScalarGridSpec(
        num_scalar_prefetch=1,
        grid=(count_blocks,),
        in_specs=[
            pl.BlockSpec((BLOCK, row_width), lambda b, img: (b, 0)),
            pl.BlockSpec(
                (kv_local, 2, row_groups, None, share_rows, HD),
                lambda b, img: (0, 0, 0, b, 0, 0),
            ),
        ],
        out_specs=pl.BlockSpec((BLOCK, row_width), lambda b, img: (b, 0)),
    )
    return pl.pallas_call(
        kernel,
        grid_spec=grid_spec,
        out_shape=jax.ShapeDtypeStruct(queries.shape, queries.dtype),
    )(block_image, queries, kv_shares)


def holder_of(image_ids, image_slot):
    image_count = image_slot.shape[0]
    same_image = image_ids[:, None] == jnp.arange(image_count, dtype=jnp.int32)[None, :]
    return jnp.sum(jnp.where(same_image, image_slot[None, :], 0), axis=1)


def local(queries, memory_kv, block_image, image_slot):
    seq_count = lax.axis_size("seq")
    own_blocks = block_image.shape[0]
    _, img_rows, kv_width = memory_kv.shape
    kv_local = kv_width // (2 * HD)
    row_groups = seq_count // (2 * kv_local)
    share_rows = img_rows // row_groups
    shares = memory_kv.reshape(row_groups, share_rows, kv_local, 2, HD)
    shares = shares.transpose(2, 3, 0, 1, 4).reshape(seq_count, share_rows, HD)
    tag = jnp.zeros((seq_count, TAG_ROWS, HD), shares.dtype)
    tag = tag.at[:, 0, :own_blocks].set(block_image.astype(shares.dtype)[None, :])
    payload = jnp.concatenate([shares, tag], axis=1)
    held = lax.all_to_all(payload, "seq", split_axis=0, concat_axis=0, tiled=True)
    wanted = held[:, share_rows, :own_blocks].astype(jnp.int32).reshape(seq_count * own_blocks)
    wanted_slot = holder_of(wanted, image_slot)
    outgoing = jnp.take(held[:, :share_rows], wanted_slot, axis=0, mode="clip")
    outgoing = outgoing.reshape(seq_count, own_blocks, share_rows, HD)
    arrived = lax.all_to_all(outgoing, "seq", split_axis=0, concat_axis=0, tiled=True)
    arrived = arrived.reshape(kv_local, 2, row_groups, own_blocks, share_rows, HD)
    return attend(queries, arrived, block_image)


def solution(mesh):
    placed = (P(("doc", "seq"), None), P(("doc", "seq"), None, None), P(("doc", "seq")), P("doc"))
    return jax.shard_map(
        local, mesh=mesh, in_specs=placed, out_specs=P(("doc", "seq"), None), check_vma=False
    )
```

```python
import functools

import jax
import jax.numpy as jnp
from jax import lax
from jax.experimental import pallas as pl
from jax.experimental.pallas import tpu as pltpu
from jax.sharding import PartitionSpec as P

HD = 128
KV_HEADS = 4
BLOCK = 128
TAG_ROWS = 16
LOG2E = 1.4426950408889634


def attend_head(q_ref, k, v, o_ref, valid, col0, group_size):
    q = jnp.concatenate(
        [q_ref[:, col0 + g * HD:col0 + (g + 1) * HD] for g in range(group_size)], axis=0
    )
    s = lax.dot_general(k, q, (((1,), (1,)), ((), ())), preferred_element_type=jnp.float32)
    m = jnp.max(s, axis=0, keepdims=True)
    w = jnp.exp2((s - m) * (HD ** (-0.5) * LOG2E))
    inv = 1.0 / jnp.sum(w, axis=0, keepdims=True)
    p = (w * inv).astype(jnp.bfloat16)
    ctx = lax.dot_general(p, v, (((0,), (0,)), ((), ())), preferred_element_type=jnp.float32)
    ctx = jnp.where(valid, ctx, 0.0).astype(o_ref.dtype)
    for g in range(group_size):
        o_ref[:, col0 + g * HD:col0 + (g + 1) * HD] = ctx[g * BLOCK:(g + 1) * BLOCK]


def attend_kernel(image_ref, q_ref, kv_ref, o_ref, *, group_size, kv_local, memory_rows):
    b = pl.program_id(0)
    valid = image_ref[b] >= 0
    for j in range(kv_local):
        k = kv_ref[j, 0].reshape(memory_rows, HD)
        v = kv_ref[j, 1].reshape(memory_rows, HD)
        attend_head(q_ref, k, v, o_ref, valid, j * group_size * HD, group_size)


def attend(queries, kv_shares, block_image):
    row_count, row_width = queries.shape
    kv_local, _, row_groups, count_blocks, share_rows, _ = kv_shares.shape
    group_size = row_width // (HD * kv_local)
    kernel = functools.partial(
        attend_kernel, group_size=group_size, kv_local=kv_local,
        memory_rows=row_groups * share_rows,
    )
    grid_spec = pltpu.PrefetchScalarGridSpec(
        num_scalar_prefetch=1,
        grid=(count_blocks,),
        in_specs=[
            pl.BlockSpec((BLOCK, row_width), lambda b, img: (b, 0)),
            pl.BlockSpec(
                (kv_local, 2, row_groups, None, share_rows, HD),
                lambda b, img: (0, 0, 0, b, 0, 0),
            ),
        ],
        out_specs=pl.BlockSpec((BLOCK, row_width), lambda b, img: (b, 0)),
    )
    return pl.pallas_call(
        kernel,
        grid_spec=grid_spec,
        out_shape=jax.ShapeDtypeStruct(queries.shape, queries.dtype),
    )(block_image, queries, kv_shares)


def pack_kernel(image_ref, kv_ref, out_ref, *, row_groups, share_rows, parts, own_blocks):
    row = lax.broadcasted_iota(jnp.int32, (TAG_ROWS, HD), 0)
    lane = lax.broadcasted_iota(jnp.int32, (TAG_ROWS, HD), 1)
    tag = jnp.zeros((TAG_ROWS, HD), jnp.float32)
    for i in range(own_blocks):
        tag = jnp.where((row == 0) & (lane == i), image_ref[i].astype(jnp.float32), tag)
    tag = tag.astype(out_ref.dtype)
    for part in range(parts):
        for rg in range(row_groups):
            c = part * row_groups + rg
            out_ref[c, :share_rows, :] = kv_ref[rg * share_rows:(rg + 1) * share_rows, part * HD:(part + 1) * HD]
            out_ref[c, share_rows:, :] = tag


def pack_shares(memory_kv, block_image, row_groups, share_rows):
    _, img_rows, kv_width = memory_kv.shape
    parts = kv_width // HD
    count = parts * row_groups
    kernel = functools.partial(
        pack_kernel, row_groups=row_groups, share_rows=share_rows, parts=parts,
        own_blocks=block_image.shape[0],
    )
    grid_spec = pltpu.PrefetchScalarGridSpec(
        num_scalar_prefetch=1,
        grid=(1,),
        in_specs=[pl.BlockSpec((None, img_rows, kv_width), lambda i, img: (0, 0, 0))],
        out_specs=pl.BlockSpec((count, share_rows + TAG_ROWS, HD), lambda i, img: (0, 0, 0)),
    )
    return pl.pallas_call(
        kernel,
        grid_spec=grid_spec,
        out_shape=jax.ShapeDtypeStruct((count, share_rows + TAG_ROWS, HD), memory_kv.dtype),
    )(block_image, memory_kv)


def holder_of(image_ids, image_slot):
    image_count = image_slot.shape[0]
    same_image = image_ids[:, None] == jnp.arange(image_count, dtype=jnp.int32)[None, :]
    return jnp.sum(jnp.where(same_image, image_slot[None, :], 0), axis=1)


def local(queries, memory_kv, block_image, image_slot):
    seq_count = lax.axis_size("seq")
    own_blocks = block_image.shape[0]
    _, img_rows, kv_width = memory_kv.shape
    kv_local = kv_width // (2 * HD)
    row_groups = seq_count // (2 * kv_local)
    share_rows = img_rows // row_groups
    payload = pack_shares(memory_kv, block_image, row_groups, share_rows)
    held = lax.all_to_all(payload, "seq", split_axis=0, concat_axis=0, tiled=True)
    wanted = held[:, share_rows, :own_blocks].astype(jnp.int32).reshape(seq_count * own_blocks)
    wanted_slot = holder_of(wanted, image_slot)
    outgoing = jnp.take(held[:, :share_rows], wanted_slot, axis=0, mode="clip")
    outgoing = outgoing.reshape(seq_count, own_blocks, share_rows, HD)
    arrived = lax.all_to_all(outgoing, "seq", split_axis=0, concat_axis=0, tiled=True)
    arrived = arrived.reshape(kv_local, 2, row_groups, own_blocks, share_rows, HD)
    return attend(queries, arrived, block_image)


def solution(mesh):
    placed = (P(("doc", "seq"), None), P(("doc", "seq"), None, None), P(("doc", "seq")), P("doc"))
    return jax.shard_map(
        local, mesh=mesh, in_specs=placed, out_specs=P(("doc", "seq"), None), check_vma=False
    )
```

```python
import functools

import jax
import jax.numpy as jnp
from jax import lax
from jax.experimental import pallas as pl
from jax.experimental.pallas import tpu as pltpu
from jax.sharding import PartitionSpec as P

HD = 128
KV_HEADS = 4
BLOCK = 128
TAG_ROWS = 16
LOG2E = 1.4426950408889634


def attend_head(q_ref, k, v, o_ref, valid, col0, group_size):
    q = jnp.concatenate(
        [q_ref[:, col0 + g * HD:col0 + (g + 1) * HD] for g in range(group_size)], axis=0
    )
    s = lax.dot_general(k, q, (((1,), (1,)), ((), ())), preferred_element_type=jnp.float32)
    m = jnp.max(s, axis=0, keepdims=True)
    w = jnp.exp2((s - m) * (HD ** (-0.5) * LOG2E))
    inv = 1.0 / jnp.sum(w, axis=0, keepdims=True)
    p = (w * inv).astype(jnp.bfloat16)
    ctx = lax.dot_general(p, v, (((0,), (0,)), ((), ())), preferred_element_type=jnp.float32)
    ctx = jnp.where(valid, ctx, 0.0).astype(o_ref.dtype)
    for g in range(group_size):
        o_ref[:, col0 + g * HD:col0 + (g + 1) * HD] = ctx[g * BLOCK:(g + 1) * BLOCK]


def attend_kernel(image_ref, q_ref, kv_ref, *refs, group_size, kv_local, memory_rows, first):
    o_ref = refs[-1]
    b = pl.program_id(0) + first
    valid = image_ref[b] >= 0
    for j in range(kv_local):
        k = kv_ref[j, 0].reshape(memory_rows, HD)
        v = kv_ref[j, 1].reshape(memory_rows, HD)
        attend_head(q_ref, k, v, o_ref, valid, j * group_size * HD, group_size)


def attend(queries, kv_shares, block_image, first, previous=None):
    row_count, row_width = queries.shape
    kv_local, _, row_groups, count_blocks, share_rows, _ = kv_shares.shape
    group_size = row_width // (HD * kv_local)
    kernel = functools.partial(
        attend_kernel, group_size=group_size, kv_local=kv_local,
        memory_rows=row_groups * share_rows, first=first,
    )
    in_specs = [
        pl.BlockSpec((BLOCK, row_width), lambda b, img: (b + first, 0)),
        pl.BlockSpec(
            (kv_local, 2, row_groups, None, share_rows, HD),
            lambda b, img: (0, 0, 0, b, 0, 0),
        ),
    ]
    operands = [block_image, queries, kv_shares]
    aliases = {}
    if previous is not None:
        in_specs.append(pl.BlockSpec(memory_space=pl.ANY))
        operands.append(previous)
        aliases = {3: 0}
    grid_spec = pltpu.PrefetchScalarGridSpec(
        num_scalar_prefetch=1,
        grid=(count_blocks,),
        in_specs=in_specs,
        out_specs=pl.BlockSpec((BLOCK, row_width), lambda b, img: (b + first, 0)),
    )
    return pl.pallas_call(
        kernel,
        grid_spec=grid_spec,
        out_shape=jax.ShapeDtypeStruct(queries.shape, queries.dtype),
        input_output_aliases=aliases,
    )(*operands)


def holder_of(image_ids, image_slot):
    image_count = image_slot.shape[0]
    same_image = image_ids[:, None] == jnp.arange(image_count, dtype=jnp.int32)[None, :]
    return jnp.sum(jnp.where(same_image, image_slot[None, :], 0), axis=1)


def local(queries, memory_kv, block_image, image_slot):
    seq_count = lax.axis_size("seq")
    own_blocks = block_image.shape[0]
    _, img_rows, kv_width = memory_kv.shape
    kv_local = kv_width // (2 * HD)
    row_groups = seq_count // (2 * kv_local)
    share_rows = img_rows // row_groups
    shares = memory_kv.reshape(row_groups, share_rows, kv_local, 2, HD)
    shares = shares.transpose(2, 3, 0, 1, 4).reshape(seq_count, share_rows, HD)
    tag = jnp.zeros((seq_count, TAG_ROWS, HD), shares.dtype)
    tag = tag.at[:, 0, :own_blocks].set(block_image.astype(shares.dtype)[None, :])
    payload = jnp.concatenate([shares, tag], axis=1)
    held = lax.all_to_all(payload, "seq", split_axis=0, concat_axis=0, tiled=True)
    wanted = held[:, share_rows, :own_blocks].astype(jnp.int32).reshape(seq_count * own_blocks)
    wanted_slot = holder_of(wanted, image_slot)
    outgoing = jnp.take(held[:, :share_rows], wanted_slot, axis=0, mode="clip")
    outgoing = outgoing.reshape(seq_count, own_blocks, share_rows, HD)
    split = own_blocks - 1
    early = lax.all_to_all(outgoing[:, :split], "seq", split_axis=0, concat_axis=0, tiled=True)
    late = lax.all_to_all(outgoing[:, split:], "seq", split_axis=0, concat_axis=0, tiled=True)
    early = early.reshape(kv_local, 2, row_groups, split, share_rows, HD)
    late = late.reshape(kv_local, 2, row_groups, own_blocks - split, share_rows, HD)
    result = attend(queries, early, block_image, 0)
    return attend(queries, late, block_image, split, result)


def solution(mesh):
    placed = (P(("doc", "seq"), None), P(("doc", "seq"), None, None), P(("doc", "seq")), P("doc"))
    return jax.shard_map(
        local, mesh=mesh, in_specs=placed, out_specs=P(("doc", "seq"), None), check_vma=False
    )
```

```python
import functools

import jax
import jax.numpy as jnp
from jax import lax
from jax.experimental import pallas as pl
from jax.experimental.pallas import tpu as pltpu
from jax.sharding import PartitionSpec as P

HD = 128
KV_HEADS = 4
BLOCK = 128
TAG_ROWS = 16
LOG2E = 1.4426950408889634


def attend_head(q_ref, k, v, o_ref, valid, col0, group_size):
    q = jnp.concatenate(
        [q_ref[:, col0 + g * HD:col0 + (g + 1) * HD] for g in range(group_size)], axis=0
    )
    s = lax.dot_general(k, q, (((1,), (1,)), ((), ())), preferred_element_type=jnp.float32)
    m = jnp.max(s, axis=0, keepdims=True)
    w = jnp.exp2((s - m) * (HD ** (-0.5) * LOG2E))
    inv = 1.0 / jnp.sum(w, axis=0, keepdims=True)
    p = (w * inv).astype(jnp.bfloat16)
    ctx = lax.dot_general(p, v, (((0,), (0,)), ((), ())), preferred_element_type=jnp.float32)
    ctx = jnp.where(valid, ctx, 0.0).astype(o_ref.dtype)
    for g in range(group_size):
        o_ref[:, col0 + g * HD:col0 + (g + 1) * HD] = ctx[g * BLOCK:(g + 1) * BLOCK]


def attend_kernel(image_ref, q_ref, kv_ref, *refs, group_size, kv_local, memory_rows, first):
    o_ref = refs[-1]
    b = pl.program_id(0) + first
    valid = image_ref[b] >= 0
    for j in range(kv_local):
        k = kv_ref[j, 0].reshape(memory_rows, HD)
        v = kv_ref[j, 1].reshape(memory_rows, HD)
        attend_head(q_ref, k, v, o_ref, valid, j * group_size * HD, group_size)


def attend(queries, kv_shares, block_image, first, previous=None):
    row_count, row_width = queries.shape
    kv_local, _, row_groups, count_blocks, share_rows, _ = kv_shares.shape
    group_size = row_width // (HD * kv_local)
    kernel = functools.partial(
        attend_kernel, group_size=group_size, kv_local=kv_local,
        memory_rows=row_groups * share_rows, first=first,
    )
    in_specs = [
        pl.BlockSpec((BLOCK, row_width), lambda b, img: (b + first, 0)),
        pl.BlockSpec(
            (kv_local, 2, row_groups, None, share_rows, HD),
            lambda b, img: (0, 0, 0, b, 0, 0),
        ),
    ]
    operands = [block_image, queries, kv_shares]
    aliases = {}
    if previous is not None:
        in_specs.append(pl.BlockSpec(memory_space=pl.ANY))
        operands.append(previous)
        aliases = {3: 0}
    grid_spec = pltpu.PrefetchScalarGridSpec(
        num_scalar_prefetch=1,
        grid=(count_blocks,),
        in_specs=in_specs,
        out_specs=pl.BlockSpec((BLOCK, row_width), lambda b, img: (b + first, 0)),
    )
    return pl.pallas_call(
        kernel,
        grid_spec=grid_spec,
        out_shape=jax.ShapeDtypeStruct(queries.shape, queries.dtype),
        input_output_aliases=aliases,
    )(*operands)


def holder_of(image_ids, image_slot):
    image_count = image_slot.shape[0]
    same_image = image_ids[:, None] == jnp.arange(image_count, dtype=jnp.int32)[None, :]
    return jnp.sum(jnp.where(same_image, image_slot[None, :], 0), axis=1)


def local(queries, memory_kv, block_image, image_slot):
    seq_count = lax.axis_size("seq")
    own_blocks = block_image.shape[0]
    _, img_rows, kv_width = memory_kv.shape
    kv_local = kv_width // (2 * HD)
    row_groups = seq_count // (2 * kv_local)
    share_rows = img_rows // row_groups
    shares = memory_kv.reshape(row_groups, share_rows, kv_local, 2, HD)
    shares = shares.transpose(2, 3, 0, 1, 4).reshape(seq_count, share_rows, HD)
    tag = jnp.zeros((seq_count, TAG_ROWS, HD), shares.dtype)
    tag = tag.at[:, 0, :own_blocks].set(block_image.astype(shares.dtype)[None, :])
    payload = jnp.concatenate([shares, tag], axis=1)
    held = lax.all_to_all(payload, "seq", split_axis=0, concat_axis=0, tiled=True)
    wanted = held[:, share_rows, :own_blocks].astype(jnp.int32).reshape(seq_count * own_blocks)
    wanted_slot = holder_of(wanted, image_slot)
    split = own_blocks - 1
    wanted_slot = wanted_slot.reshape(seq_count, own_blocks)
    source = held[:, :share_rows]
    early = jnp.take(source, wanted_slot[:, :split].reshape(-1), axis=0, mode="clip")
    late = jnp.take(source, wanted_slot[:, split:].reshape(-1), axis=0, mode="clip")
    early = early.reshape(seq_count, split, share_rows, HD)
    late = late.reshape(seq_count, own_blocks - split, share_rows, HD)
    early = lax.all_to_all(early, "seq", split_axis=0, concat_axis=0, tiled=True)
    late = lax.all_to_all(late, "seq", split_axis=0, concat_axis=0, tiled=True)
    early = early.reshape(kv_local, 2, row_groups, split, share_rows, HD)
    late = late.reshape(kv_local, 2, row_groups, own_blocks - split, share_rows, HD)
    result = attend(queries, early, block_image, 0)
    return attend(queries, late, block_image, split, result)


def solution(mesh):
    placed = (P(("doc", "seq"), None), P(("doc", "seq"), None, None), P(("doc", "seq")), P("doc"))
    return jax.shard_map(
        local, mesh=mesh, in_specs=placed, out_specs=P(("doc", "seq"), None), check_vma=False
    )
```

```python
import functools

import jax
import jax.numpy as jnp
from jax import lax
from jax.experimental import pallas as pl
from jax.experimental.pallas import tpu as pltpu
from jax.sharding import PartitionSpec as P

HD = 128
KV_HEADS = 4
BLOCK = 128
TAG_ROWS = 16
LOG2E = 1.4426950408889634


def attend_head(q_ref, k, v, o_ref, valid, col0, group_size):
    q = jnp.concatenate(
        [q_ref[:, col0 + g * HD:col0 + (g + 1) * HD] for g in range(group_size)], axis=0
    )
    s = lax.dot_general(k, q, (((1,), (1,)), ((), ())), preferred_element_type=jnp.float32)
    m = jnp.max(s, axis=0, keepdims=True)
    w = jnp.exp2((s - m) * (HD ** (-0.5) * LOG2E))
    inv = 1.0 / jnp.sum(w, axis=0, keepdims=True)
    p = (w * inv).astype(jnp.bfloat16)
    ctx = lax.dot_general(p, v, (((0,), (0,)), ((), ())), preferred_element_type=jnp.float32)
    ctx = jnp.where(valid, ctx, 0.0).astype(o_ref.dtype)
    for g in range(group_size):
        o_ref[:, col0 + g * HD:col0 + (g + 1) * HD] = ctx[g * BLOCK:(g + 1) * BLOCK]


def attend_kernel(image_ref, q_ref, kv_ref, *refs, group_size, kv_local, memory_rows, first):
    o_ref = refs[-1]
    b = pl.program_id(0) + first
    valid = image_ref[b] >= 0
    for j in range(kv_local):
        k = kv_ref[j, 0].reshape(memory_rows, HD)
        v = kv_ref[j, 1].reshape(memory_rows, HD)
        attend_head(q_ref, k, v, o_ref, valid, j * group_size * HD, group_size)


def attend(queries, kv_shares, block_image, first, heads_per_step, previous=None):
    row_count, row_width = queries.shape
    kv_local, _, row_groups, count_blocks, share_rows, _ = kv_shares.shape
    group_size = row_width // (HD * kv_local)
    step_cols = heads_per_step * group_size * HD
    kernel = functools.partial(
        attend_kernel, group_size=group_size, kv_local=heads_per_step,
        memory_rows=row_groups * share_rows, first=first,
    )
    in_specs = [
        pl.BlockSpec((BLOCK, step_cols), lambda b, h, img: (b + first, h)),
        pl.BlockSpec(
            (heads_per_step, 2, row_groups, None, share_rows, HD),
            lambda b, h, img: (h, 0, 0, b, 0, 0),
        ),
    ]
    operands = [block_image, queries, kv_shares]
    aliases = {}
    if previous is not None:
        in_specs.append(pl.BlockSpec(memory_space=pl.ANY))
        operands.append(previous)
        aliases = {3: 0}
    grid_spec = pltpu.PrefetchScalarGridSpec(
        num_scalar_prefetch=1,
        grid=(count_blocks, kv_local // heads_per_step),
        in_specs=in_specs,
        out_specs=pl.BlockSpec((BLOCK, step_cols), lambda b, h, img: (b + first, h)),
    )
    return pl.pallas_call(
        kernel,
        grid_spec=grid_spec,
        out_shape=jax.ShapeDtypeStruct(queries.shape, queries.dtype),
        input_output_aliases=aliases,
    )(*operands)


def holder_of(image_ids, image_slot):
    image_count = image_slot.shape[0]
    same_image = image_ids[:, None] == jnp.arange(image_count, dtype=jnp.int32)[None, :]
    return jnp.sum(jnp.where(same_image, image_slot[None, :], 0), axis=1)


def local(queries, memory_kv, block_image, image_slot):
    seq_count = lax.axis_size("seq")
    own_blocks = block_image.shape[0]
    _, img_rows, kv_width = memory_kv.shape
    kv_local = kv_width // (2 * HD)
    row_groups = seq_count // (2 * kv_local)
    share_rows = img_rows // row_groups
    shares = memory_kv.reshape(row_groups, share_rows, kv_local, 2, HD)
    shares = shares.transpose(2, 3, 0, 1, 4).reshape(seq_count, share_rows, HD)
    tag = jnp.zeros((seq_count, TAG_ROWS, HD), shares.dtype)
    tag = tag.at[:, 0, :own_blocks].set(block_image.astype(shares.dtype)[None, :])
    payload = jnp.concatenate([shares, tag], axis=1)
    held = lax.all_to_all(payload, "seq", split_axis=0, concat_axis=0, tiled=True)
    wanted = held[:, share_rows, :own_blocks].astype(jnp.int32).reshape(seq_count * own_blocks)
    wanted_slot = holder_of(wanted, image_slot)
    split = own_blocks - 1
    wanted_slot = wanted_slot.reshape(seq_count, own_blocks)
    source = held[:, :share_rows]
    early = jnp.take(source, wanted_slot[:, :split].reshape(-1), axis=0, mode="clip")
    late = jnp.take(source, wanted_slot[:, split:].reshape(-1), axis=0, mode="clip")
    early = early.reshape(seq_count, split, share_rows, HD)
    late = late.reshape(seq_count, own_blocks - split, share_rows, HD)
    early = lax.all_to_all(early, "seq", split_axis=0, concat_axis=0, tiled=True)
    late = lax.all_to_all(late, "seq", split_axis=0, concat_axis=0, tiled=True)
    early = early.reshape(kv_local, 2, row_groups, split, share_rows, HD)
    late = late.reshape(kv_local, 2, row_groups, own_blocks - split, share_rows, HD)
    result = attend(queries, early, block_image, 0, kv_local)
    return attend(queries, late, block_image, split, 1, result)


def solution(mesh):
    placed = (P(("doc", "seq"), None), P(("doc", "seq"), None, None), P(("doc", "seq")), P("doc"))
    return jax.shard_map(
        local, mesh=mesh, in_specs=placed, out_specs=P(("doc", "seq"), None), check_vma=False
    )
```

```python
import functools

import jax
import jax.numpy as jnp
from jax import lax
from jax.experimental import pallas as pl
from jax.experimental.pallas import tpu as pltpu
from jax.sharding import PartitionSpec as P

HD = 128
KV_HEADS = 4
BLOCK = 128
TAG_ROWS = 16
LOG2E = 1.4426950408889634


def attend_head(q_ref, k, v, o_ref, valid, col0, group_size):
    q = jnp.concatenate(
        [q_ref[:, col0 + g * HD:col0 + (g + 1) * HD] for g in range(group_size)], axis=0
    )
    s = lax.dot_general(k, q, (((1,), (1,)), ((), ())), preferred_element_type=jnp.float32)
    m = jnp.max(s, axis=0, keepdims=True)
    w = jnp.exp2((s - m) * (HD ** (-0.5) * LOG2E))
    inv = 1.0 / jnp.sum(w, axis=0, keepdims=True)
    p = (w * inv).astype(jnp.bfloat16)
    ctx = lax.dot_general(p, v, (((0,), (0,)), ((), ())), preferred_element_type=jnp.float32)
    ctx = jnp.where(valid, ctx, 0.0).astype(o_ref.dtype)
    for g in range(group_size):
        o_ref[:, col0 + g * HD:col0 + (g + 1) * HD] = ctx[g * BLOCK:(g + 1) * BLOCK]


def attend_kernel(image_ref, q_ref, kv_ref, *refs, group_size, kv_local, memory_rows, first):
    o_ref = refs[-1]
    b = pl.program_id(0) + first
    valid = image_ref[b] >= 0
    for j in range(kv_local):
        k = kv_ref[j, 0].reshape(memory_rows, HD)
        v = kv_ref[j, 1].reshape(memory_rows, HD)
        attend_head(q_ref, k, v, o_ref, valid, j * group_size * HD, group_size)


def attend(queries, kv_shares, block_image, first, previous=None):
    row_count, row_width = queries.shape
    kv_local, _, row_groups, count_blocks, share_rows, _ = kv_shares.shape
    group_size = row_width // (HD * kv_local)
    kernel = functools.partial(
        attend_kernel, group_size=group_size, kv_local=kv_local,
        memory_rows=row_groups * share_rows, first=first,
    )
    in_specs = [
        pl.BlockSpec((BLOCK, row_width), lambda b, img: (b + first, 0)),
        pl.BlockSpec(
            (kv_local, 2, row_groups, None, share_rows, HD),
            lambda b, img: (0, 0, 0, b, 0, 0),
        ),
    ]
    operands = [block_image, queries, kv_shares]
    aliases = {}
    if previous is not None:
        in_specs.append(pl.BlockSpec(memory_space=pl.ANY))
        operands.append(previous)
        aliases = {3: 0}
    grid_spec = pltpu.PrefetchScalarGridSpec(
        num_scalar_prefetch=1,
        grid=(count_blocks,),
        in_specs=in_specs,
        out_specs=pl.BlockSpec((BLOCK, row_width), lambda b, img: (b + first, 0)),
    )
    return pl.pallas_call(
        kernel,
        grid_spec=grid_spec,
        out_shape=jax.ShapeDtypeStruct(queries.shape, queries.dtype),
        input_output_aliases=aliases,
    )(*operands)


def attend_late(queries, kv_shares, block_image, first, previous):
    row_count, row_width = queries.shape
    kv_local, _, row_groups, count_blocks, share_rows, _ = kv_shares.shape
    group_size = row_width // (HD * kv_local)
    q_late = lax.slice_in_dim(queries, first * BLOCK, (first + count_blocks) * BLOCK, axis=0)
    kernel = functools.partial(
        attend_kernel, group_size=group_size, kv_local=kv_local,
        memory_rows=row_groups * share_rows, first=first,
    )
    grid_spec = pltpu.PrefetchScalarGridSpec(
        num_scalar_prefetch=1,
        grid=(count_blocks,),
        in_specs=[
            pl.BlockSpec(memory_space=pltpu.VMEM),
            pl.BlockSpec(memory_space=pltpu.VMEM),
            pl.BlockSpec(memory_space=pl.ANY),
        ],
        out_specs=pl.BlockSpec((BLOCK, row_width), lambda b, img: (b + first, 0)),
    )
    return pl.pallas_call(
        kernel,
        grid_spec=grid_spec,
        out_shape=jax.ShapeDtypeStruct(queries.shape, queries.dtype),
        input_output_aliases={3: 0},
    )(block_image, q_late, kv_shares.reshape(kv_local, 2, row_groups * count_blocks, share_rows, HD), previous)


def holder_of(image_ids, image_slot):
    image_count = image_slot.shape[0]
    same_image = image_ids[:, None] == jnp.arange(image_count, dtype=jnp.int32)[None, :]
    return jnp.sum(jnp.where(same_image, image_slot[None, :], 0), axis=1)


def local(queries, memory_kv, block_image, image_slot):
    seq_count = lax.axis_size("seq")
    own_blocks = block_image.shape[0]
    _, img_rows, kv_width = memory_kv.shape
    kv_local = kv_width // (2 * HD)
    row_groups = seq_count // (2 * kv_local)
    share_rows = img_rows // row_groups
    shares = memory_kv.reshape(row_groups, share_rows, kv_local, 2, HD)
    shares = shares.transpose(2, 3, 0, 1, 4).reshape(seq_count, share_rows, HD)
    tag = jnp.zeros((seq_count, TAG_ROWS, HD), shares.dtype)
    tag = tag.at[:, 0, :own_blocks].set(block_image.astype(shares.dtype)[None, :])
    payload = jnp.concatenate([shares, tag], axis=1)
    held = lax.all_to_all(payload, "seq", split_axis=0, concat_axis=0, tiled=True)
    wanted = held[:, share_rows, :own_blocks].astype(jnp.int32).reshape(seq_count * own_blocks)
    wanted_slot = holder_of(wanted, image_slot)
    split = own_blocks - 1
    wanted_slot = wanted_slot.reshape(seq_count, own_blocks)
    source = held[:, :share_rows]
    early = jnp.take(source, wanted_slot[:, :split].reshape(-1), axis=0, mode="clip")
    late = jnp.take(source, wanted_slot[:, split:].reshape(-1), axis=0, mode="clip")
    early = early.reshape(seq_count, split, share_rows, HD)
    late = late.reshape(seq_count, own_blocks - split, share_rows, HD)
    early = lax.all_to_all(early, "seq", split_axis=0, concat_axis=0, tiled=True)
    late = lax.all_to_all(late, "seq", split_axis=0, concat_axis=0, tiled=True)
    early = early.reshape(kv_local, 2, row_groups, split, share_rows, HD)
    late = late.reshape(kv_local, 2, row_groups, own_blocks - split, share_rows, HD)
    result = attend(queries, early, block_image, 0)
    return attend_late(queries, late, block_image, split, result)


def solution(mesh):
    placed = (P(("doc", "seq"), None), P(("doc", "seq"), None, None), P(("doc", "seq")), P("doc"))
    return jax.shard_map(
        local, mesh=mesh, in_specs=placed, out_specs=P(("doc", "seq"), None), check_vma=False
    )
```

```python
import functools

import jax
import jax.numpy as jnp
from jax import lax
from jax.experimental import pallas as pl
from jax.experimental.pallas import tpu as pltpu
from jax.sharding import PartitionSpec as P

HD = 128
KV_HEADS = 4
BLOCK = 128
TAG_ROWS = 16
LOG2E = 1.4426950408889634


def attend_head(q_ref, k, v, o_ref, valid, col0, group_size):
    q = jnp.concatenate(
        [q_ref[:, col0 + g * HD:col0 + (g + 1) * HD] for g in range(group_size)], axis=0
    )
    s = lax.dot_general(k, q, (((1,), (1,)), ((), ())), preferred_element_type=jnp.float32)
    m = jnp.max(s, axis=0, keepdims=True)
    w = jnp.exp2((s - m) * (HD ** (-0.5) * LOG2E))
    inv = 1.0 / jnp.sum(w, axis=0, keepdims=True)
    p = (w * inv).astype(jnp.bfloat16)
    ctx = lax.dot_general(p, v, (((0,), (0,)), ((), ())), preferred_element_type=jnp.float32)
    ctx = jnp.where(valid, ctx, 0.0).astype(o_ref.dtype)
    for g in range(group_size):
        o_ref[:, col0 + g * HD:col0 + (g + 1) * HD] = ctx[g * BLOCK:(g + 1) * BLOCK]


def attend_kernel(image_ref, q_ref, kv_ref, *refs, group_size, kv_local, memory_rows, first):
    o_ref = refs[-1]
    b = pl.program_id(0) + first
    valid = image_ref[b] >= 0
    for j in range(kv_local):
        k = kv_ref[j, 0].reshape(memory_rows, HD)
        v = kv_ref[j, 1].reshape(memory_rows, HD)
        attend_head(q_ref, k, v, o_ref, valid, j * group_size * HD, group_size)


def attend(queries, kv_shares, block_image, first, previous=None):
    row_count, row_width = queries.shape
    kv_local, _, row_groups, count_blocks, share_rows, _ = kv_shares.shape
    group_size = row_width // (HD * kv_local)
    kernel = functools.partial(
        attend_kernel, group_size=group_size, kv_local=kv_local,
        memory_rows=row_groups * share_rows, first=first,
    )
    in_specs = [
        pl.BlockSpec((BLOCK, row_width), lambda b, img: (b + first, 0)),
        pl.BlockSpec(
            (kv_local, 2, row_groups, None, share_rows, HD),
            lambda b, img: (0, 0, 0, b, 0, 0),
        ),
    ]
    operands = [block_image, queries, kv_shares]
    aliases = {}
    if previous is not None:
        in_specs.append(pl.BlockSpec(memory_space=pl.ANY))
        operands.append(previous)
        aliases = {3: 0}
    grid_spec = pltpu.PrefetchScalarGridSpec(
        num_scalar_prefetch=1,
        grid=(count_blocks,),
        in_specs=in_specs,
        out_specs=pl.BlockSpec((BLOCK, row_width), lambda b, img: (b + first, 0)),
    )
    return pl.pallas_call(
        kernel,
        grid_spec=grid_spec,
        out_shape=jax.ShapeDtypeStruct(queries.shape, queries.dtype),
        input_output_aliases=aliases,
    )(*operands)


def attend_late(queries, kv_shares, block_image, first, previous):
    row_count, row_width = queries.shape
    kv_local, _, row_groups, count_blocks, share_rows, _ = kv_shares.shape
    group_size = row_width // (HD * kv_local)
    q_late = lax.slice_in_dim(queries, first * BLOCK, (first + count_blocks) * BLOCK, axis=0)
    kernel = functools.partial(
        attend_kernel, group_size=group_size, kv_local=kv_local,
        memory_rows=row_groups * share_rows, first=first,
    )
    grid_spec = pltpu.PrefetchScalarGridSpec(
        num_scalar_prefetch=1,
        grid=(count_blocks,),
        in_specs=[
            pl.BlockSpec(memory_space=pltpu.VMEM),
            pl.BlockSpec(memory_space=pltpu.VMEM),
            pl.BlockSpec(memory_space=pl.ANY),
        ],
        out_specs=pl.BlockSpec((BLOCK, row_width), lambda b, img: (b + first, 0)),
    )
    return pl.pallas_call(
        kernel,
        grid_spec=grid_spec,
        out_shape=jax.ShapeDtypeStruct(queries.shape, queries.dtype),
        input_output_aliases={3: 0},
    )(block_image, q_late, kv_shares.reshape(kv_local, 2, row_groups * count_blocks, share_rows, HD), previous)


def pack_kernel(image_ref, kv_ref, out_ref, *, row_groups, share_rows, parts, own_blocks):
    row = lax.broadcasted_iota(jnp.int32, (TAG_ROWS, HD), 0)
    lane = lax.broadcasted_iota(jnp.int32, (TAG_ROWS, HD), 1)
    tag = jnp.zeros((TAG_ROWS, HD), jnp.float32)
    for i in range(own_blocks):
        tag = jnp.where((row == 0) & (lane == i), image_ref[i].astype(jnp.float32), tag)
    tag = tag.astype(out_ref.dtype)
    for part in range(parts):
        for rg in range(row_groups):
            c = part * row_groups + rg
            out_ref[c, :share_rows, :] = kv_ref[rg * share_rows:(rg + 1) * share_rows, part * HD:(part + 1) * HD]
            out_ref[c, share_rows:, :] = tag


def pack_shares(memory_kv, block_image, row_groups, share_rows):
    _, img_rows, kv_width = memory_kv.shape
    parts = kv_width // HD
    count = parts * row_groups
    kernel = functools.partial(
        pack_kernel, row_groups=row_groups, share_rows=share_rows, parts=parts,
        own_blocks=block_image.shape[0],
    )
    grid_spec = pltpu.PrefetchScalarGridSpec(
        num_scalar_prefetch=1,
        grid=(1,),
        in_specs=[pl.BlockSpec((None, img_rows, kv_width), lambda i, img: (0, 0, 0))],
        out_specs=pl.BlockSpec((count, share_rows + TAG_ROWS, HD), lambda i, img: (0, 0, 0)),
    )
    return pl.pallas_call(
        kernel,
        grid_spec=grid_spec,
        out_shape=jax.ShapeDtypeStruct((count, share_rows + TAG_ROWS, HD), memory_kv.dtype),
    )(block_image, memory_kv)


def holder_of(image_ids, image_slot):
    image_count = image_slot.shape[0]
    same_image = image_ids[:, None] == jnp.arange(image_count, dtype=jnp.int32)[None, :]
    return jnp.sum(jnp.where(same_image, image_slot[None, :], 0), axis=1)


def local(queries, memory_kv, block_image, image_slot):
    seq_count = lax.axis_size("seq")
    own_blocks = block_image.shape[0]
    _, img_rows, kv_width = memory_kv.shape
    kv_local = kv_width // (2 * HD)
    row_groups = seq_count // (2 * kv_local)
    share_rows = img_rows // row_groups
    payload = pack_shares(memory_kv, block_image, row_groups, share_rows)
    held = lax.all_to_all(payload, "seq", split_axis=0, concat_axis=0, tiled=True)
    wanted = held[:, share_rows, :own_blocks].astype(jnp.int32).reshape(seq_count * own_blocks)
    wanted_slot = holder_of(wanted, image_slot)
    split = own_blocks - 1
    wanted_slot = wanted_slot.reshape(seq_count, own_blocks)
    source = held[:, :share_rows]
    early = jnp.take(source, wanted_slot[:, :split].reshape(-1), axis=0, mode="clip")
    late = jnp.take(source, wanted_slot[:, split:].reshape(-1), axis=0, mode="clip")
    early = early.reshape(seq_count, split, share_rows, HD)
    late = late.reshape(seq_count, own_blocks - split, share_rows, HD)
    early = lax.all_to_all(early, "seq", split_axis=0, concat_axis=0, tiled=True)
    late = lax.all_to_all(late, "seq", split_axis=0, concat_axis=0, tiled=True)
    early = early.reshape(kv_local, 2, row_groups, split, share_rows, HD)
    late = late.reshape(kv_local, 2, row_groups, own_blocks - split, share_rows, HD)
    result = attend(queries, early, block_image, 0)
    return attend_late(queries, late, block_image, split, result)


def solution(mesh):
    placed = (P(("doc", "seq"), None), P(("doc", "seq"), None, None), P(("doc", "seq")), P("doc"))
    return jax.shard_map(
        local, mesh=mesh, in_specs=placed, out_specs=P(("doc", "seq"), None), check_vma=False
    )
```

```python
import functools

import jax
import jax.numpy as jnp
from jax import lax
from jax.experimental import pallas as pl
from jax.experimental.pallas import tpu as pltpu
from jax.sharding import PartitionSpec as P

HD = 128
KV_HEADS = 4
BLOCK = 128
TAG_ROWS = 16
LOG2E = 1.4426950408889634


def attend_head(q_ref, k, v, o_ref, valid, col0, group_size):
    q = jnp.concatenate(
        [q_ref[:, col0 + g * HD:col0 + (g + 1) * HD] for g in range(group_size)], axis=0
    )
    s = lax.dot_general(k, q, (((1,), (1,)), ((), ())), preferred_element_type=jnp.float32)
    m = jnp.max(s, axis=0, keepdims=True)
    w = jnp.exp2((s - m) * (HD ** (-0.5) * LOG2E))
    inv = 1.0 / jnp.sum(w, axis=0, keepdims=True)
    p = (w * inv).astype(jnp.bfloat16)
    ctx = lax.dot_general(p, v, (((0,), (0,)), ((), ())), preferred_element_type=jnp.float32)
    ctx = jnp.where(valid, ctx, 0.0).astype(o_ref.dtype)
    for g in range(group_size):
        o_ref[:, col0 + g * HD:col0 + (g + 1) * HD] = ctx[g * BLOCK:(g + 1) * BLOCK]


def attend_kernel(image_ref, q_ref, kv_ref, *refs, group_size, kv_local, memory_rows, first):
    o_ref = refs[-1]
    b = pl.program_id(0) + first
    valid = image_ref[b] >= 0
    for j in range(kv_local):
        k = kv_ref[j, 0].reshape(memory_rows, HD)
        v = kv_ref[j, 1].reshape(memory_rows, HD)
        attend_head(q_ref, k, v, o_ref, valid, j * group_size * HD, group_size)


def attend(queries, kv_shares, block_image, first, heads_per_step, previous=None):
    row_count, row_width = queries.shape
    kv_local, _, row_groups, count_blocks, share_rows, _ = kv_shares.shape
    group_size = row_width // (HD * kv_local)
    step_cols = heads_per_step * group_size * HD
    kernel = functools.partial(
        attend_kernel, group_size=group_size, kv_local=heads_per_step,
        memory_rows=row_groups * share_rows, first=first,
    )
    in_specs = [
        pl.BlockSpec((BLOCK, step_cols), lambda b, h, img: (b + first, h)),
        pl.BlockSpec(
            (heads_per_step, 2, row_groups, None, share_rows, HD),
            lambda b, h, img: (h, 0, 0, b, 0, 0),
        ),
    ]
    operands = [block_image, queries, kv_shares]
    aliases = {}
    if previous is not None:
        in_specs.append(pl.BlockSpec(memory_space=pl.ANY))
        operands.append(previous)
        aliases = {3: 0}
    grid_spec = pltpu.PrefetchScalarGridSpec(
        num_scalar_prefetch=1,
        grid=(count_blocks, kv_local // heads_per_step),
        in_specs=in_specs,
        out_specs=pl.BlockSpec((BLOCK, step_cols), lambda b, h, img: (b + first, h)),
    )
    return pl.pallas_call(
        kernel,
        grid_spec=grid_spec,
        out_shape=jax.ShapeDtypeStruct(queries.shape, queries.dtype),
        input_output_aliases=aliases,
    )(*operands)


def holder_of(image_ids, image_slot):
    image_count = image_slot.shape[0]
    same_image = image_ids[:, None] == jnp.arange(image_count, dtype=jnp.int32)[None, :]
    return jnp.sum(jnp.where(same_image, image_slot[None, :], 0), axis=1)


def local(queries, memory_kv, block_image, image_slot):
    seq_count = lax.axis_size("seq")
    own_blocks = block_image.shape[0]
    _, img_rows, kv_width = memory_kv.shape
    kv_local = kv_width // (2 * HD)
    row_groups = seq_count // (2 * kv_local)
    share_rows = img_rows // row_groups
    shares = memory_kv.reshape(row_groups, share_rows, kv_local, 2, HD)
    shares = shares.transpose(2, 3, 0, 1, 4).reshape(seq_count, share_rows, HD)
    tag = jnp.zeros((seq_count, TAG_ROWS, HD), shares.dtype)
    tag = tag.at[:, 0, :own_blocks].set(block_image.astype(shares.dtype)[None, :])
    payload = jnp.concatenate([shares, tag], axis=1)
    held = lax.all_to_all(payload, "seq", split_axis=0, concat_axis=0, tiled=True)
    wanted = held[:, share_rows, :own_blocks].astype(jnp.int32).reshape(seq_count * own_blocks)
    wanted_slot = holder_of(wanted, image_slot)
    split = own_blocks - 1
    wanted_slot = wanted_slot.reshape(seq_count, own_blocks)
    source = held[:, :share_rows]
    early = jnp.take(source, wanted_slot[:, :split].reshape(-1), axis=0, mode="clip")
    late = jnp.take(source, wanted_slot[:, split:].reshape(-1), axis=0, mode="clip")
    early = early.reshape(seq_count, split, share_rows, HD)
    late = late.reshape(seq_count, own_blocks - split, share_rows, HD)
    early = lax.all_to_all(early, "seq", split_axis=0, concat_axis=0, tiled=True)
    late = lax.all_to_all(late, "seq", split_axis=0, concat_axis=0, tiled=True)
    early = early.reshape(kv_local, 2, row_groups, split, share_rows, HD)
    late = late.reshape(kv_local, 2, row_groups, own_blocks - split, share_rows, HD)
    result = attend(queries, early, block_image, 0, kv_local)
    return attend(queries, late, block_image, split, kv_local // 2, result)


def solution(mesh):
    placed = (P(("doc", "seq"), None), P(("doc", "seq"), None, None), P(("doc", "seq")), P("doc"))
    return jax.shard_map(
        local, mesh=mesh, in_specs=placed, out_specs=P(("doc", "seq"), None), check_vma=False
    )
```
